256 devices in a mesh: seg: 8 (over y, core), sec: 32 (over x, z).
Axes of the slice: x: 4, y: 4, z: 8, core: 2. Of those that a mesh axis runs over, the one named last changes fastest.
Arguments:
- psi_init: float32 [8, 32, 256, 256], P('seg', 'sec'), may hold values from -6 to 6
- boundary_env: float32 [32, 18, 256, 256], P('sec')
- right_env: float32 [8, 32, 18, 256, 256], P('seg', 'sec')
- transfer_blocks: float32 [8, 32, 256, 256], P('seg', 'sec')
- transfer_mix: float32 [8, 18, 18], P('seg')
- hop_left: float32 [8, 32, 256, 256], P('seg', 'sec'), may hold values from -0.75 to 0.75
- hop_right: float32 [8, 32, 256, 256], P('seg', 'sec'), may hold values from -0.75 to 0.75
- block_sizes: int32 [8, 2, 32], P('seg'), may hold values from 64 to 256, as said below
- sources: int32 [8, 32], P('seg'), may hold values from 0 to 31, each once within a row
Outputs:
- state: float32 [8, 32, 256, 256], P('seg', 'sec')
The draws below stay inside these ranges and needn't reach their ends.
Inputs may be any that keep to these rules, and one draw needn't show every extreme that they name: `sources`: each block number appears once in a segment's list. `block_sizes`: each segment has a block with 256 live rows and one with 256 live columns.
All inputs are finite; a program needn't handle non-finite values.
Results may differ from the reference program's by a relative error of at most 0.0003.
Values sent between devices are 32-bit elements; how exact they have to be, the bound alone decides.
No kernel may reach another device: no remote copies, remote signals or barrier semaphores. Data moves between devices by JAX's collectives and lax.ppermute only.
A program may use at most 128 MiB of HBM per device.

```python
import jax
import jax.numpy as jnp
from jax import lax

P_SIZE = 256
W = 18
DAV = 2
BLK = 32
SEGS = 8


def env_law(key, shape):
    key_diag, key_rest = jax.random.split(key)
    rows = lax.broadcasted_iota(jnp.int32, shape, len(shape) - 2)
    cols = lax.broadcasted_iota(jnp.int32, shape, len(shape) - 1)
    unit = (rows == cols).astype(jnp.float32)
    diag_vals = jax.random.uniform(key_diag, shape[:-1], jnp.float32, 0.5, 2.0)
    noise = jax.random.normal(key_rest, shape, jnp.float32) * (0.5 / P_SIZE ** 0.5)
    return diag_vals[..., :, None] * unit + noise


def near_unit(key, shape, spread):
    rows = lax.broadcasted_iota(jnp.int32, shape, len(shape) - 2)
    cols = lax.broadcasted_iota(jnp.int32, shape, len(shape) - 1)
    unit = (rows == cols).astype(jnp.float32)
    return unit + jax.random.normal(key, shape, jnp.float32) * (spread / shape[-1] ** 0.5)


def draw_boundary_env(key, part):
    return env_law(jax.random.fold_in(key, 11), (BLK, W, P_SIZE, P_SIZE))


def draw_right_env(key, part):
    return env_law(jax.random.fold_in(key, 12), (SEGS, BLK, W, P_SIZE, P_SIZE))


def draw_transfer_blocks(key, part):
    return near_unit(jax.random.fold_in(key, 13), (SEGS, BLK, P_SIZE, P_SIZE), 0.3)


def draw_transfer_mix(key, part):
    return near_unit(jax.random.fold_in(key, 14), (SEGS, W, W), 0.3)


def draw_block_sizes(key, part):
    key_vals, key_pick = jax.random.split(jax.random.fold_in(key, 15))
    values = jax.random.randint(key_vals, (SEGS, 2, BLK), P_SIZE // 4, P_SIZE + 1)
    chosen = jax.random.randint(key_pick, (SEGS, 2, 1), 0, BLK)
    filled = lax.broadcasted_iota(jnp.int32, (SEGS, 2, BLK), 2) == chosen
    return jnp.where(filled, P_SIZE, values).astype(jnp.int32)


def block_levels(rng, extent, shards, smallest, top_value):
    loudness, own = 1.0, jax.random.fold_in(rng, 6)
    for position, blocks in shards:
        heights = jnp.exp(jax.random.uniform(jax.random.fold_in(own, position), (blocks,), jnp.float32, smallest / len(shards), top_value / len(shards)))
        loudness = loudness * jnp.repeat(heights, extent[position] // blocks).reshape([-1 if axis == position else 1 for axis in range(len(extent))])
    return loudness


def normal_values(stream_key, extent, scale, reach, shards=(), held_as=jnp.bfloat16):
    array = scale * jax.random.normal(stream_key, extent, jnp.float32)
    if shards:
        array = array * block_levels(stream_key, extent, shards, -0.22, 0.18)
    return jnp.clip(array, -reach, reach).astype(held_as)


def setup_inputs(seed: int = 0) -> dict:
    splits = jax.random.split(jax.random.key(seed), 10)
    psi_init = normal_values(splits[0], (SEGS, BLK, P_SIZE, P_SIZE), 1.0, 6.0, ((0, 8), (1, 32)), jnp.float32)
    boundary_env = draw_boundary_env(jax.random.fold_in(splits[9], 71), 0)
    right_env = draw_right_env(jax.random.fold_in(splits[9], 71), 0)
    transfer_blocks = draw_transfer_blocks(jax.random.fold_in(splits[9], 71), 0)
    transfer_mix = draw_transfer_mix(jax.random.fold_in(splits[9], 71), 0)
    hop_left = normal_values(splits[5], (SEGS, BLK, P_SIZE, P_SIZE), (P_SIZE // 4) ** -0.5, 0.75, ((0, 8), (1, 32)), jnp.float32)
    hop_right = normal_values(splits[6], (SEGS, BLK, P_SIZE, P_SIZE), (P_SIZE // 4) ** -0.5, 0.75, ((0, 8), (1, 32)), jnp.float32)
    block_sizes = draw_block_sizes(jax.random.fold_in(splits[9], 71), 0)
    sources = jax.vmap(lambda own: jax.random.permutation(own, BLK))(jax.random.split(splits[8], SEGS)).reshape((SEGS, BLK)).astype(jnp.int32)
    return dict(psi_init=psi_init, boundary_env=boundary_env, right_env=right_env, transfer_blocks=transfer_blocks, transfer_mix=transfer_mix, hop_left=hop_left, hop_right=hop_right, block_sizes=block_sizes, sources=sources)


HIGH = lax.Precision.HIGHEST
EPSILON = 1e-06

def product(left, right):
    return jnp.matmul(left, right, precision=HIGH)

def build_env(prefix_mix, prefix_blocks, boundary):
    turned = product(product(jnp.swapaxes(prefix_blocks, 1, 2)[:, None], boundary), prefix_blocks[:, None])
    return jnp.einsum('vw,bvij->bwij', prefix_mix, turned, precision=HIGH)

def solve_window(initial, left_env, right_side, left_hop, right_hop, live_sizes, source_list):
    block_width = initial.shape[-1]
    places = lax.broadcasted_iota(jnp.int32, (1, block_width), 1)
    row_live = (places < live_sizes[0][:, None]).astype(jnp.float32)
    col_live = (places < live_sizes[1][:, None]).astype(jnp.float32)
    masking = row_live[:, :, None] * col_live[:, None, :]
    diagonal = jnp.einsum('bwi,bwj->bij', jnp.diagonal(left_env, axis1=2, axis2=3), jnp.diagonal(right_side, axis1=2, axis2=3), precision=HIGH)

    def apply_h(vector):
        local_part = lax.optimization_barrier(jnp.sum(product(product(left_env, vector[:, None]), right_side), axis=1))
        regrouped = product(vector, right_hop)[source_list]
        return masking * (local_part + product(left_hop, regrouped))
    vector = masking * initial
    vector = vector / jnp.sqrt(jnp.sum(vector * vector) + EPSILON)
    for turn_index in range(DAV):
        image_vec = apply_h(vector)
        rayleigh = jnp.sum(vector * image_vec)
        residue = image_vec - rayleigh * vector
        shifted = diagonal - rayleigh
        update = vector - residue * shifted / (shifted * shifted + 1.0)
        vector = update / jnp.sqrt(jnp.sum(update * update) + EPSILON)
    return vector * jnp.sqrt(jnp.float32(BLK * P_SIZE * P_SIZE))

def reference(psi_init, boundary_env, right_env, transfer_blocks, transfer_mix, hop_left, hop_right, block_sizes, sources):
    prefix_mix = jnp.eye(W, dtype=jnp.float32)
    prefix_blocks = jnp.broadcast_to(jnp.eye(P_SIZE, dtype=jnp.float32), (BLK, P_SIZE, P_SIZE))
    results = []
    for segment in range(SEGS):
        left_env = build_env(prefix_mix, prefix_blocks, boundary_env)
        results.append(solve_window(psi_init[segment], left_env, right_env[segment], hop_left[segment], hop_right[segment], block_sizes[segment], sources[segment]))
        prefix_mix = product(prefix_mix, transfer_mix[segment])
        prefix_blocks = product(prefix_blocks, transfer_blocks[segment])
    return jnp.stack(results)
```

```python
import jax
import jax.numpy as jnp
from jax import lax
from jax.sharding import PartitionSpec as P

DAV = 2


HIGH = lax.Precision.HIGHEST
EPSILON = 1e-06


def passed_along(value, axis, steps):
    count = lax.axis_size(axis)
    initial, last = (max(0, -steps), min(count, count - steps))
    return lax.ppermute(value, axis, [(source, source + steps) for source in range(initial, last)])


def product(left, right):
    return jnp.matmul(left, right, precision=HIGH)


def sec_total(values):
    count = lax.axis_size("sec")
    spread = jnp.broadcast_to(values[None, :], (count, values.shape[0]))
    return jnp.sum(lax.all_to_all(spread, "sec", 0, 0, tiled=True), axis=0)


def regroup(moving, wanted):
    count = lax.axis_size("sec")
    rows, cols = moving.shape
    pieces = moving.reshape(count, rows // count, cols)
    held = lax.all_to_all(pieces, "sec", 0, 0, tiled=True)
    ordered = jnp.take(held, wanted, axis=0, mode="clip")
    back = lax.all_to_all(ordered, "sec", 0, 0, tiled=True)
    return back.reshape(rows, cols)


def prefix_scan(own_mix, own_blocks):
    seg = lax.axis_index("seg")
    count = lax.axis_size("seg")
    width = own_blocks.shape[0]
    channels = own_mix.shape[0]
    pad = -(-channels // 8) * 8
    eye_mix = jnp.eye(channels, dtype=jnp.float32)
    eye_blocks = jnp.eye(width, dtype=jnp.float32)
    span_mix, span_blocks = own_mix, own_blocks
    before_mix, before_blocks = eye_mix, eye_blocks
    step = 1
    while step < count:
        packed = jnp.concatenate(
            [span_blocks, jnp.pad(span_mix, ((0, pad - channels), (0, width - channels)))], axis=0
        )
        got = passed_along(packed, "seg", step)
        got_blocks = got[:width]
        got_mix = got[width:width + channels, :channels]
        take = seg >= step
        if step == 1:
            before_mix = jnp.where(take, got_mix, eye_mix)
            before_blocks = jnp.where(take, got_blocks, eye_blocks)
        else:
            before_mix = jnp.where(take, product(got_mix, before_mix), before_mix)
            before_blocks = jnp.where(take, product(got_blocks, before_blocks), before_blocks)
        if step * 2 < count:
            span_mix = jnp.where(take, product(got_mix, span_mix), span_mix)
            span_blocks = jnp.where(take, product(got_blocks, span_blocks), span_blocks)
        step *= 2
    return before_mix, before_blocks


def per_device(
    psi_init,
    boundary_env,
    right_env,
    transfer_blocks,
    transfer_mix,
    hop_left,
    hop_right,
    block_sizes,
    sources,
):
    initial = psi_init[0, 0]
    boundary = boundary_env[0]
    right_side = right_env[0, 0]
    own_blocks = transfer_blocks[0, 0]
    own_mix = transfer_mix[0]
    left_hop = hop_left[0, 0]
    right_hop = hop_right[0, 0]
    all_sizes = block_sizes[0]
    all_sources = sources[0]
    block_width = initial.shape[1]
    sector_count = lax.axis_size("sec")
    me = lax.axis_index("sec")

    places = lax.broadcasted_iota(jnp.int32, (block_width,), 0)
    row_live = (places < all_sizes[0, me]).astype(jnp.float32)
    col_live = (places < all_sizes[1, me]).astype(jnp.float32)
    masking = row_live[:, None] * col_live[None, :]

    first = masking * initial
    first_moved = regroup(product(first, right_hop), all_sources)

    prefix_mix, prefix_blocks = prefix_scan(own_mix, own_blocks)
    half = jnp.einsum("ukl,lj->ukj", boundary, prefix_blocks, precision=HIGH)
    turned = jnp.einsum("ki,ukj->uij", prefix_blocks, half, precision=HIGH)
    left_env = jnp.einsum("uw,uij->wij", prefix_mix, turned, precision=HIGH)
    diagonal = jnp.einsum(
        "wi,wj->ij",
        jnp.diagonal(left_env, axis1=1, axis2=2),
        jnp.diagonal(right_side, axis1=1, axis2=2),
        precision=HIGH,
    )

    def apply_h(vector, moved):
        inner = jnp.einsum("wij,jk->wik", left_env, vector, precision=HIGH)
        local_part = jnp.einsum("wik,wkl->il", inner, right_side, precision=HIGH)
        return masking * (local_part + product(left_hop, moved))

    def step(vector, image_vec, rayleigh):
        residue = image_vec - rayleigh * vector
        shifted = diagonal - rayleigh
        return vector - residue * shifted / (shifted * shifted + 1.0)

    image = apply_h(first, first_moved)
    sums = sec_total(jnp.stack([jnp.sum(first * first), jnp.sum(first * image)]))
    scale = 1.0 / jnp.sqrt(sums[0] + EPSILON)
    vector = first * scale
    image_vec = image * scale
    rayleigh = sums[1] / (sums[0] + EPSILON)
    for turn_index in range(1, DAV):
        update = step(vector, image_vec, rayleigh)
        moved = regroup(product(update, right_hop), all_sources)
        image = apply_h(update, moved)
        sums = sec_total(jnp.stack([jnp.sum(update * update), jnp.sum(update * image)]))
        scale = 1.0 / jnp.sqrt(sums[0] + EPSILON)
        vector = update * scale
        image_vec = image * scale
        rayleigh = sums[1] / (sums[0] + EPSILON)
    update = step(vector, image_vec, rayleigh)
    total = sec_total(jnp.sum(update * update)[None])[0]
    cells = float(sector_count * block_width * block_width)
    return (update * (jnp.sqrt(jnp.float32(cells)) / jnp.sqrt(total + EPSILON)))[None, None]


def solution(mesh):
    return jax.shard_map(
        per_device,
        mesh=mesh,
        in_specs=(
            P("seg", "sec", None, None),
            P("sec", None, None, None),
            P("seg", "sec", None, None, None),
            P("seg", "sec", None, None),
            P("seg", None, None),
            P("seg", "sec", None, None),
            P("seg", "sec", None, None),
            P("seg", None, None),
            P("seg", None),
        ),
        out_specs=P("seg", "sec", None, None),
        check_vma=False,
    )
```

```python
import jax
import jax.numpy as jnp
from jax import lax
from jax.sharding import PartitionSpec as P

DAV = 2


HIGH = lax.Precision.HIGHEST
EPSILON = 1e-06


def passed_along(value, axis, steps):
    count = lax.axis_size(axis)
    initial, last = (max(0, -steps), min(count, count - steps))
    return lax.ppermute(value, axis, [(source, source + steps) for source in range(initial, last)])


def product(left, right):
    return jnp.matmul(left, right, precision=HIGH)


def sec_total(values):
    count = lax.axis_size("sec")
    spread = jnp.broadcast_to(values[None, :], (count, values.shape[0]))
    return jnp.sum(lax.all_to_all(spread, "sec", 0, 0, tiled=True), axis=0)


def regroup(moving, wanted):
    count = lax.axis_size("sec")
    rows, cols = moving.shape
    pieces = moving.reshape(count, rows // count, cols)
    held = lax.all_to_all(pieces, "sec", 0, 0, tiled=True)
    ordered = jnp.take(held, wanted, axis=0, mode="clip")
    back = lax.all_to_all(ordered, "sec", 0, 0, tiled=True)
    return back.reshape(rows, cols)


def prefix_scan(own_mix, own_blocks):
    seg = lax.axis_index("seg")
    count = lax.axis_size("seg")
    width = own_blocks.shape[0]
    channels = own_mix.shape[0]
    pad = -(-channels // 8) * 8
    eye_mix = jnp.eye(channels, dtype=jnp.float32)
    eye_blocks = jnp.eye(width, dtype=jnp.float32)
    span_mix, span_blocks = own_mix, own_blocks
    before_mix, before_blocks = eye_mix, eye_blocks
    step = 1
    while step < count:
        packed = jnp.concatenate(
            [span_blocks, jnp.pad(span_mix, ((0, pad - channels), (0, width - channels)))], axis=0
        )
        got = passed_along(packed, "seg", step)
        got_blocks = got[:width]
        got_mix = got[width:width + channels, :channels]
        take = seg >= step
        if step == 1:
            before_mix = jnp.where(take, got_mix, eye_mix)
            before_blocks = jnp.where(take, got_blocks, eye_blocks)
        else:
            before_mix = jnp.where(take, product(got_mix, before_mix), before_mix)
            before_blocks = jnp.where(take, product(got_blocks, before_blocks), before_blocks)
        if step * 2 < count:
            span_mix = jnp.where(take, product(got_mix, span_mix), span_mix)
            span_blocks = jnp.where(take, product(got_blocks, span_blocks), span_blocks)
        step *= 2
    return before_mix, before_blocks


def per_device(
    psi_init,
    boundary_env,
    right_env,
    transfer_blocks,
    transfer_mix,
    hop_left,
    hop_right,
    block_sizes,
    sources,
):
    initial = psi_init[0, 0]
    boundary = boundary_env[0]
    right_side = right_env[0, 0]
    own_blocks = transfer_blocks[0, 0]
    own_mix = transfer_mix[0]
    left_hop = hop_left[0, 0]
    right_hop = hop_right[0, 0]
    all_sizes = block_sizes[0]
    all_sources = sources[0]
    block_width = initial.shape[1]
    sector_count = lax.axis_size("sec")
    me = lax.axis_index("sec")

    places = lax.broadcasted_iota(jnp.int32, (block_width,), 0)
    row_live = (places < all_sizes[0, me]).astype(jnp.float32)
    col_live = (places < all_sizes[1, me]).astype(jnp.float32)
    masking = row_live[:, None] * col_live[None, :]

    first = masking * initial
    first_moved = regroup(product(first, right_hop), all_sources)

    eye_lanes = (places[:, None] == places[None, :]).astype(jnp.float32)
    right_diag = jnp.sum(right_side * eye_lanes, axis=2)
    prefix_mix, prefix_blocks = prefix_scan(own_mix, own_blocks)
    mixed = jnp.einsum("uw,ukl->wkl", prefix_mix, boundary, precision=HIGH)
    half = jnp.einsum("wkl,lj->wkj", mixed, prefix_blocks, precision=HIGH)
    left_env = jnp.einsum("ki,wkj->iwj", prefix_blocks, half, precision=HIGH)
    left_diag = jnp.sum(prefix_blocks[None] * half, axis=1)
    diagonal = jnp.einsum("wi,wj->ij", left_diag, right_diag, precision=HIGH)

    def apply_h(vector, moved):
        inner = jnp.einsum("iwj,jk->iwk", left_env, vector, precision=HIGH)
        local_part = jnp.einsum("iwk,wkl->il", inner, right_side, precision=HIGH)
        return masking * (local_part + product(left_hop, moved))

    def step(vector, image_vec, rayleigh):
        residue = image_vec - rayleigh * vector
        shifted = diagonal - rayleigh
        return vector - residue * shifted / (shifted * shifted + 1.0)

    image = apply_h(first, first_moved)
    sums = sec_total(jnp.stack([jnp.sum(first * first), jnp.sum(first * image)]))
    scale = 1.0 / jnp.sqrt(sums[0] + EPSILON)
    vector = first * scale
    image_vec = image * scale
    rayleigh = sums[1] / (sums[0] + EPSILON)
    for turn_index in range(1, DAV):
        update = step(vector, image_vec, rayleigh)
        moved = regroup(product(update, right_hop), all_sources)
        image = apply_h(update, moved)
        sums = sec_total(jnp.stack([jnp.sum(update * update), jnp.sum(update * image)]))
        scale = 1.0 / jnp.sqrt(sums[0] + EPSILON)
        vector = update * scale
        image_vec = image * scale
        rayleigh = sums[1] / (sums[0] + EPSILON)
    update = step(vector, image_vec, rayleigh)
    total = sec_total(jnp.sum(update * update)[None])[0]
    cells = float(sector_count * block_width * block_width)
    return (update * (jnp.sqrt(jnp.float32(cells)) / jnp.sqrt(total + EPSILON)))[None, None]


def solution(mesh):
    return jax.shard_map(
        per_device,
        mesh=mesh,
        in_specs=(
            P("seg", "sec", None, None),
            P("sec", None, None, None),
            P("seg", "sec", None, None, None),
            P("seg", "sec", None, None),
            P("seg", None, None),
            P("seg", "sec", None, None),
            P("seg", "sec", None, None),
            P("seg", None, None),
            P("seg", None),
        ),
        out_specs=P("seg", "sec", None, None),
        check_vma=False,
    )
```

```python
import jax
import jax.numpy as jnp
from jax import lax
from jax.sharding import PartitionSpec as P

DAV = 2


HIGH = lax.Precision.HIGHEST
EPSILON = 1e-06


def passed_along(value, axis, steps):
    count = lax.axis_size(axis)
    initial, last = (max(0, -steps), min(count, count - steps))
    return lax.ppermute(value, axis, [(source, source + steps) for source in range(initial, last)])


def product(left, right):
    return jnp.matmul(left, right, precision=HIGH)


def sec_total(values):
    count = lax.axis_size("sec")
    spread = jnp.broadcast_to(values[None, :], (count, values.shape[0]))
    return jnp.sum(lax.all_to_all(spread, "sec", 0, 0, tiled=True), axis=0)


def regroup(blocks, wanted, partial=None):
    count = lax.axis_size("sec")
    rows, cols = blocks[0].shape
    per = rows // count
    parts = [block.reshape(count, per, cols) for block in blocks]
    if partial is not None:
        row = jnp.pad(partial, (0, cols - partial.shape[0]))
        parts.append(jnp.broadcast_to(row[None, None, :], (count, 1, cols)))
    held = lax.all_to_all(jnp.concatenate(parts, axis=1), "sec", 0, 0, tiled=True)
    data = len(blocks) * per
    ordered = jnp.take(held[:, :data], wanted, axis=0, mode="clip")
    back = lax.all_to_all(ordered, "sec", 0, 0, tiled=True)
    got = [back[:, i * per:(i + 1) * per].reshape(rows, cols) for i in range(len(blocks))]
    if partial is None:
        return got
    return got, jnp.sum(held[:, data, :partial.shape[0]], axis=0)


def prefix_scan(own_mix, own_blocks):
    seg = lax.axis_index("seg")
    count = lax.axis_size("seg")
    width = own_blocks.shape[0]
    channels = own_mix.shape[0]
    pad = -(-channels // 8) * 8
    eye_mix = jnp.eye(channels, dtype=jnp.float32)
    eye_blocks = jnp.eye(width, dtype=jnp.float32)
    span_mix, span_blocks = own_mix, own_blocks
    before_mix, before_blocks = eye_mix, eye_blocks
    step = 1
    while step < count:
        packed = jnp.concatenate(
            [span_blocks, jnp.pad(span_mix, ((0, pad - channels), (0, width - channels)))], axis=0
        )
        got = passed_along(packed, "seg", step)
        got_blocks = got[:width]
        got_mix = got[width:width + channels, :channels]
        take = seg >= step
        if step == 1:
            before_mix = jnp.where(take, got_mix, eye_mix)
            before_blocks = jnp.where(take, got_blocks, eye_blocks)
        else:
            before_mix = jnp.where(take, product(got_mix, before_mix), before_mix)
            before_blocks = jnp.where(take, product(got_blocks, before_blocks), before_blocks)
        if step * 2 < count:
            span_mix = jnp.where(take, product(got_mix, span_mix), span_mix)
            span_blocks = jnp.where(take, product(got_blocks, span_blocks), span_blocks)
        step *= 2
    return before_mix, before_blocks


def per_device(
    psi_init,
    boundary_env,
    right_env,
    transfer_blocks,
    transfer_mix,
    hop_left,
    hop_right,
    block_sizes,
    sources,
):
    initial = psi_init[0, 0]
    boundary = boundary_env[0]
    right_side = right_env[0, 0]
    own_blocks = transfer_blocks[0, 0]
    own_mix = transfer_mix[0]
    left_hop = hop_left[0, 0]
    right_hop = hop_right[0, 0]
    all_sizes = block_sizes[0]
    all_sources = sources[0]
    block_width = initial.shape[1]
    sector_count = lax.axis_size("sec")
    me = lax.axis_index("sec")

    places = lax.broadcasted_iota(jnp.int32, (block_width,), 0)
    row_live = (places < all_sizes[0, me]).astype(jnp.float32)
    col_live = (places < all_sizes[1, me]).astype(jnp.float32)
    masking = row_live[:, None] * col_live[None, :]

    first = masking * initial
    first_src, right_hop_src = regroup([first, right_hop], all_sources)
    first_moved = product(first_src, right_hop_src)

    eye_lanes = (places[:, None] == places[None, :]).astype(jnp.float32)
    right_diag = jnp.sum(right_side * eye_lanes, axis=2)
    prefix_mix, prefix_blocks = prefix_scan(own_mix, own_blocks)
    mixed = jnp.einsum("uw,ukl->wkl", prefix_mix, boundary, precision=HIGH)
    half = jnp.einsum("wkl,lj->wkj", mixed, prefix_blocks, precision=HIGH)
    left_env = jnp.einsum("ki,wkj->iwj", prefix_blocks, half, precision=HIGH)
    left_diag = jnp.sum(prefix_blocks[None] * half, axis=1)
    diagonal = jnp.einsum("wi,wj->ij", left_diag, right_diag, precision=HIGH)

    def apply_h(vector, moved):
        inner = jnp.einsum("iwj,jk->iwk", left_env, vector, precision=HIGH)
        local_part = jnp.einsum("iwk,wkl->il", inner, right_side, precision=HIGH)
        return masking * (local_part + product(left_hop, moved))

    def step(vector, image_vec, rayleigh, diag):
        residue = image_vec - rayleigh * vector
        shifted = diag - rayleigh
        return vector - residue * shifted / (shifted * shifted + 1.0)

    image = apply_h(first, first_moved)
    partial = jnp.stack([jnp.sum(first * first), jnp.sum(first * image)])
    vector, vector_src = first, first_src
    diag_src = None
    for turn_index in range(DAV):
        last = turn_index == DAV - 1
        if last:
            sums = sec_total(partial)
        elif diag_src is None:
            (image_src, diag_src), sums = regroup([image, diagonal], all_sources, partial)
        else:
            (image_src,), sums = regroup([image], all_sources, partial)
        scale = 1.0 / jnp.sqrt(sums[0] + EPSILON)
        rayleigh = sums[1] / (sums[0] + EPSILON)
        update = step(vector * scale, image * scale, rayleigh, diagonal)
        if not last:
            update_src = step(vector_src * scale, image_src * scale, rayleigh, diag_src)
            image = apply_h(update, product(update_src, right_hop_src))
            partial = jnp.stack([jnp.sum(update * update), jnp.sum(update * image)])
            vector, vector_src = update, update_src
    total = sec_total(jnp.sum(update * update)[None])[0]
    cells = float(sector_count * block_width * block_width)
    return (update * (jnp.sqrt(jnp.float32(cells)) / jnp.sqrt(total + EPSILON)))[None, None]


def solution(mesh):
    return jax.shard_map(
        per_device,
        mesh=mesh,
        in_specs=(
            P("seg", "sec", None, None),
            P("sec", None, None, None),
            P("seg", "sec", None, None, None),
            P("seg", "sec", None, None),
            P("seg", None, None),
            P("seg", "sec", None, None),
            P("seg", "sec", None, None),
            P("seg", None, None),
            P("seg", None),
        ),
        out_specs=P("seg", "sec", None, None),
        check_vma=False,
    )
```

```python
import jax
import jax.numpy as jnp
from jax import lax
from jax.sharding import PartitionSpec as P

DAV = 2


HIGH = lax.Precision.HIGHEST
EPSILON = 1e-06


def passed_along(value, axis, steps):
    count = lax.axis_size(axis)
    initial, last = (max(0, -steps), min(count, count - steps))
    return lax.ppermute(value, axis, [(source, source + steps) for source in range(initial, last)])


def product(left, right):
    return jnp.matmul(left, right, precision=HIGH)


def sec_total(values):
    count = lax.axis_size("sec")
    spread = jnp.broadcast_to(values[None, :], (count, values.shape[0]))
    return jnp.sum(lax.all_to_all(spread, "sec", 0, 0, tiled=True), axis=0)


def regroup(blocks, wanted, partial=None):
    count = lax.axis_size("sec")
    rows, cols = blocks[0].shape
    per = rows // count
    parts = [block.reshape(count, per, cols) for block in blocks]
    data = len(blocks) * per
    if partial is not None:
        row = jnp.pad(partial, (0, cols - partial.shape[0]))
        parts.append(jnp.broadcast_to(row[None, None, :], (count, per, cols)))
    held = lax.all_to_all(jnp.concatenate(parts, axis=1), "sec", 0, 0, tiled=True)
    ordered = jnp.take(held[:, :data], wanted, axis=0, mode="clip")
    back = lax.all_to_all(ordered, "sec", 0, 0, tiled=True)
    got = [back[:, i * per:(i + 1) * per].reshape(rows, cols) for i in range(len(blocks))]
    if partial is None:
        return got
    return got, jnp.sum(held[:, data, :partial.shape[0]], axis=0)


def prefix_scan(own_mix, own_blocks):
    seg = lax.axis_index("seg")
    count = lax.axis_size("seg")
    width = own_blocks.shape[0]
    channels = own_mix.shape[0]
    pad = -(-channels // 8) * 8
    eye_mix = jnp.eye(channels, dtype=jnp.float32)
    eye_blocks = jnp.eye(width, dtype=jnp.float32)
    span_mix, span_blocks = own_mix, own_blocks
    before_mix, before_blocks = eye_mix, eye_blocks
    step = 1
    while step < count:
        packed = jnp.concatenate(
            [span_blocks, jnp.pad(span_mix, ((0, pad - channels), (0, width - channels)))], axis=0
        )
        got = passed_along(packed, "seg", step)
        got_blocks = got[:width]
        got_mix = got[width:width + channels, :channels]
        take = seg >= step
        if step == 1:
            before_mix = jnp.where(take, got_mix, eye_mix)
            before_blocks = jnp.where(take, got_blocks, eye_blocks)
        else:
            before_mix = jnp.where(take, product(got_mix, before_mix), before_mix)
            before_blocks = jnp.where(take, product(got_blocks, before_blocks), before_blocks)
        if step * 2 < count:
            span_mix = jnp.where(take, product(got_mix, span_mix), span_mix)
            span_blocks = jnp.where(take, product(got_blocks, span_blocks), span_blocks)
        step *= 2
    return before_mix, before_blocks


def per_device(
    psi_init,
    boundary_env,
    right_env,
    transfer_blocks,
    transfer_mix,
    hop_left,
    hop_right,
    block_sizes,
    sources,
):
    initial = psi_init[0, 0]
    boundary = boundary_env[0]
    right_side = right_env[0, 0]
    own_blocks = transfer_blocks[0, 0]
    own_mix = transfer_mix[0]
    left_hop = hop_left[0, 0]
    right_hop = hop_right[0, 0]
    all_sizes = block_sizes[0]
    all_sources = sources[0]
    block_width = initial.shape[1]
    sector_count = lax.axis_size("sec")
    me = lax.axis_index("sec")

    places = lax.broadcasted_iota(jnp.int32, (block_width,), 0)
    row_live = (places < all_sizes[0, me]).astype(jnp.float32)
    col_live = (places < all_sizes[1, me]).astype(jnp.float32)
    masking = row_live[:, None] * col_live[None, :]

    first = masking * initial
    (first_moved,) = regroup([product(first, right_hop)], all_sources)

    eye_lanes = (places[:, None] == places[None, :]).astype(jnp.float32)
    right_diag = jnp.sum(right_side * eye_lanes, axis=2)
    prefix_mix, prefix_blocks = prefix_scan(own_mix, own_blocks)
    mixed = jnp.einsum("uw,ukl->wkl", prefix_mix, boundary, precision=HIGH)
    half = jnp.einsum("wkl,lj->wkj", mixed, prefix_blocks, precision=HIGH)
    left_env = jnp.einsum("ki,wkj->iwj", prefix_blocks, half, precision=HIGH)
    left_diag = jnp.sum(prefix_blocks[None] * half, axis=1)
    diagonal = jnp.einsum("wi,wj->ij", left_diag, right_diag, precision=HIGH)

    def apply_h(vector, moved):
        inner = jnp.einsum("iwj,jk->iwk", left_env, vector, precision=HIGH)
        local_part = jnp.einsum("iwk,wkl->il", inner, right_side, precision=HIGH)
        return masking * (local_part + product(left_hop, moved))

    def step(vector, image_vec, rayleigh, diag):
        residue = image_vec - rayleigh * vector
        shifted = diag - rayleigh
        return vector - residue * shifted / (shifted * shifted + 1.0)

    image = apply_h(first, first_moved)
    partial = jnp.stack([jnp.sum(first * first), jnp.sum(first * image)])
    vector = first
    for turn_index in range(DAV):
        last = turn_index == DAV - 1
        if last:
            sums = sec_total(partial)
        else:
            (vector_src, image_src, diag_src, right_hop_src), sums = regroup(
                [vector, image, diagonal, right_hop], all_sources, partial
            )
        scale = 1.0 / jnp.sqrt(sums[0] + EPSILON)
        rayleigh = sums[1] / (sums[0] + EPSILON)
        update = step(vector * scale, image * scale, rayleigh, diagonal)
        if not last:
            update_src = step(vector_src * scale, image_src * scale, rayleigh, diag_src)
            image = apply_h(update, product(update_src, right_hop_src))
            partial = jnp.stack([jnp.sum(update * update), jnp.sum(update * image)])
            vector = update
    total = sec_total(jnp.sum(update * update)[None])[0]
    cells = float(sector_count * block_width * block_width)
    return (update * (jnp.sqrt(jnp.float32(cells)) / jnp.sqrt(total + EPSILON)))[None, None]


def solution(mesh):
    return jax.shard_map(
        per_device,
        mesh=mesh,
        in_specs=(
            P("seg", "sec", None, None),
            P("sec", None, None, None),
            P("seg", "sec", None, None, None),
            P("seg", "sec", None, None),
            P("seg", None, None),
            P("seg", "sec", None, None),
            P("seg", "sec", None, None),
            P("seg", None, None),
            P("seg", None),
        ),
        out_specs=P("seg", "sec", None, None),
        check_vma=False,
    )
```

```python
import jax
import jax.numpy as jnp
from jax import lax
from jax.sharding import PartitionSpec as P

DAV = 2


HIGH = lax.Precision.HIGHEST
EPSILON = 1e-06


def passed_along(value, axis, steps):
    count = lax.axis_size(axis)
    initial, last = (max(0, -steps), min(count, count - steps))
    return lax.ppermute(value, axis, [(source, source + steps) for source in range(initial, last)])


def product(left, right):
    return jnp.matmul(left, right, precision=HIGH)


def sec_total(values):
    count = lax.axis_size("sec")
    spread = jnp.broadcast_to(values[None, :], (count, values.shape[0]))
    return jnp.sum(lax.all_to_all(spread, "sec", 0, 0, tiled=True), axis=0)


def regroup(moving, wanted):
    count = lax.axis_size("sec")
    rows, cols = moving.shape
    pieces = moving.reshape(count, rows // count, cols)
    held = lax.all_to_all(pieces, "sec", 0, 0, tiled=True)
    ordered = jnp.take(held, wanted, axis=0, mode="clip")
    back = lax.all_to_all(ordered, "sec", 0, 0, tiled=True)
    return back.reshape(rows, cols)


def prefix_scan(own_mix, own_blocks):
    seg = lax.axis_index("seg")
    count = lax.axis_size("seg")
    width = own_blocks.shape[0]
    channels = own_mix.shape[0]
    pad = -(-channels // 8) * 8
    eye_mix = jnp.eye(channels, dtype=jnp.float32)
    eye_blocks = jnp.eye(width, dtype=jnp.float32)
    span_mix, span_blocks = own_mix, own_blocks
    before_mix, before_blocks = eye_mix, eye_blocks
    step = 1
    while step < count:
        packed = jnp.concatenate(
            [span_blocks, jnp.pad(span_mix, ((0, pad - channels), (0, width - channels)))], axis=0
        )
        got = passed_along(packed, "seg", step)
        got_blocks = got[:width]
        got_mix = got[width:width + channels, :channels]
        take = seg >= step
        if step == 1:
            before_mix = jnp.where(take, got_mix, eye_mix)
            before_blocks = jnp.where(take, got_blocks, eye_blocks)
        else:
            before_mix = jnp.where(take, product(got_mix, before_mix), before_mix)
            before_blocks = jnp.where(take, product(got_blocks, before_blocks), before_blocks)
        if step * 2 < count:
            span_mix = jnp.where(take, product(got_mix, span_mix), span_mix)
            span_blocks = jnp.where(take, product(got_blocks, span_blocks), span_blocks)
        step *= 2
    return before_mix, before_blocks


def per_device(
    psi_init,
    boundary_env,
    right_env,
    transfer_blocks,
    transfer_mix,
    hop_left,
    hop_right,
    block_sizes,
    sources,
):
    initial = psi_init[0, 0]
    boundary = boundary_env[0]
    right_side = right_env[0, 0]
    own_blocks = transfer_blocks[0, 0]
    own_mix = transfer_mix[0]
    left_hop = hop_left[0, 0]
    right_hop = hop_right[0, 0]
    all_sizes = block_sizes[0]
    all_sources = sources[0]
    block_width = initial.shape[1]
    sector_count = lax.axis_size("sec")
    me = lax.axis_index("sec")

    places = lax.broadcasted_iota(jnp.int32, (block_width,), 0)
    row_live = (places < all_sizes[0, me]).astype(jnp.float32)
    col_live = (places < all_sizes[1, me]).astype(jnp.float32)
    masking = row_live[:, None] * col_live[None, :]

    first = masking * initial
    first_moved = regroup(product(first, right_hop), all_sources)

    eye_lanes = (places[:, None] == places[None, :]).astype(jnp.float32)
    right_diag = jnp.sum(right_side * eye_lanes, axis=2)
    prefix_mix, prefix_blocks = prefix_scan(own_mix, own_blocks)
    mixed = jnp.einsum("uw,ukl->wkl", prefix_mix, boundary, precision=HIGH)
    half = jnp.einsum("wkl,lj->wkj", mixed, prefix_blocks, precision=HIGH)
    left_env = jnp.einsum("ki,wkj->iwj", prefix_blocks, half, precision=HIGH)

    def apply_h(vector, moved):
        inner = jnp.einsum("iwj,jk->iwk", left_env, vector, precision=HIGH)
        local_part = jnp.einsum("iwk,wkl->il", inner, right_side, precision=HIGH)
        return masking * (local_part + product(left_hop, moved))

    def step(vector, image_vec, rayleigh):
        residue = image_vec - rayleigh * vector
        shifted = diagonal - rayleigh
        return vector - residue * shifted / (shifted * shifted + 1.0)

    image = apply_h(first, first_moved)
    partial = jnp.stack([jnp.sum(first * first), jnp.sum(first * image)])
    partial, held_half, held_blocks = lax.optimization_barrier((partial, half, prefix_blocks))
    sums = sec_total(partial)
    left_diag = jnp.sum(held_blocks[None] * held_half, axis=1)
    diagonal = jnp.einsum("wi,wj->ij", left_diag, right_diag, precision=HIGH)
    scale = 1.0 / jnp.sqrt(sums[0] + EPSILON)
    vector = first * scale
    image_vec = image * scale
    rayleigh = sums[1] / (sums[0] + EPSILON)
    for turn_index in range(1, DAV):
        update = step(vector, image_vec, rayleigh)
        moved = regroup(product(update, right_hop), all_sources)
        image = apply_h(update, moved)
        sums = sec_total(jnp.stack([jnp.sum(update * update), jnp.sum(update * image)]))
        scale = 1.0 / jnp.sqrt(sums[0] + EPSILON)
        vector = update * scale
        image_vec = image * scale
        rayleigh = sums[1] / (sums[0] + EPSILON)
    update = step(vector, image_vec, rayleigh)
    total = sec_total(jnp.sum(update * update)[None])[0]
    cells = float(sector_count * block_width * block_width)
    return (update * (jnp.sqrt(jnp.float32(cells)) / jnp.sqrt(total + EPSILON)))[None, None]


def solution(mesh):
    return jax.shard_map(
        per_device,
        mesh=mesh,
        in_specs=(
            P("seg", "sec", None, None),
            P("sec", None, None, None),
            P("seg", "sec", None, None, None),
            P("seg", "sec", None, None),
            P("seg", None, None),
            P("seg", "sec", None, None),
            P("seg", "sec", None, None),
            P("seg", None, None),
            P("seg", None),
        ),
        out_specs=P("seg", "sec", None, None),
        check_vma=False,
    )
```

```python
import jax
import jax.numpy as jnp
from jax import lax
from jax.sharding import PartitionSpec as P
from jax.experimental import pallas as pl
from jax.experimental.pallas import tpu as pltpu

DAV = 2


HIGH = lax.Precision.HIGHEST
EPSILON = 1e-06


def passed_along(value, axis, steps):
    count = lax.axis_size(axis)
    initial, last = (max(0, -steps), min(count, count - steps))
    return lax.ppermute(value, axis, [(source, source + steps) for source in range(initial, last)])


def product(left, right):
    return jnp.matmul(left, right, precision=HIGH)


def sec_total(values):
    count = lax.axis_size("sec")
    spread = jnp.broadcast_to(values[None, :], (count, values.shape[0]))
    return jnp.sum(lax.all_to_all(spread, "sec", 0, 0, tiled=True), axis=0)


def regroup(moving, wanted):
    count = lax.axis_size("sec")
    rows, cols = moving.shape
    pieces = moving.reshape(count, rows // count, cols)
    held = lax.all_to_all(pieces, "sec", 0, 0, tiled=True)
    ordered = jnp.take(held, wanted, axis=0, mode="clip")
    back = lax.all_to_all(ordered, "sec", 0, 0, tiled=True)
    return back.reshape(rows, cols)


def _mix_kernel(mix_ref, source_ref, out_ref):
    channels = source_ref.shape[0]
    for w in range(channels):
        acc = source_ref[0] * mix_ref[0, w]
        for u in range(1, channels):
            acc = acc + source_ref[u] * mix_ref[u, w]
        out_ref[w] = acc


def channel_mix(mix, source, rows=64):
    channels, height, width = source.shape
    return pl.pallas_call(
        _mix_kernel,
        grid=(height // rows,),
        in_specs=[
            pl.BlockSpec(memory_space=pltpu.SMEM),
            pl.BlockSpec((channels, rows, width), lambda i: (0, i, 0)),
        ],
        out_specs=pl.BlockSpec((channels, rows, width), lambda i: (0, i, 0)),
        out_shape=jax.ShapeDtypeStruct(source.shape, source.dtype),
    )(mix, source)


def prefix_scan(own_mix, own_blocks):
    seg = lax.axis_index("seg")
    count = lax.axis_size("seg")
    width = own_blocks.shape[0]
    channels = own_mix.shape[0]
    pad = -(-channels // 8) * 8
    eye_mix = jnp.eye(channels, dtype=jnp.float32)
    eye_blocks = jnp.eye(width, dtype=jnp.float32)
    span_mix, span_blocks = own_mix, own_blocks
    before_mix, before_blocks = eye_mix, eye_blocks
    step = 1
    while step < count:
        packed = jnp.concatenate(
            [span_blocks, jnp.pad(span_mix, ((0, pad - channels), (0, width - channels)))], axis=0
        )
        got = passed_along(packed, "seg", step)
        got_blocks = got[:width]
        got_mix = got[width:width + channels, :channels]
        take = seg >= step
        if step == 1:
            before_mix = jnp.where(take, got_mix, eye_mix)
            before_blocks = jnp.where(take, got_blocks, eye_blocks)
        else:
            before_mix = jnp.where(take, product(got_mix, before_mix), before_mix)
            before_blocks = jnp.where(take, product(got_blocks, before_blocks), before_blocks)
        if step * 2 < count:
            span_mix = jnp.where(take, product(got_mix, span_mix), span_mix)
            span_blocks = jnp.where(take, product(got_blocks, span_blocks), span_blocks)
        step *= 2
    return before_mix, before_blocks


def per_device(
    psi_init,
    boundary_env,
    right_env,
    transfer_blocks,
    transfer_mix,
    hop_left,
    hop_right,
    block_sizes,
    sources,
):
    initial = psi_init[0, 0]
    boundary = boundary_env[0]
    right_side = right_env[0, 0]
    own_blocks = transfer_blocks[0, 0]
    own_mix = transfer_mix[0]
    left_hop = hop_left[0, 0]
    right_hop = hop_right[0, 0]
    all_sizes = block_sizes[0]
    all_sources = sources[0]
    block_width = initial.shape[1]
    sector_count = lax.axis_size("sec")
    me = lax.axis_index("sec")

    places = lax.broadcasted_iota(jnp.int32, (block_width,), 0)
    row_live = (places < all_sizes[0, me]).astype(jnp.float32)
    col_live = (places < all_sizes[1, me]).astype(jnp.float32)
    masking = row_live[:, None] * col_live[None, :]

    first = masking * initial
    first_moved = regroup(product(first, right_hop), all_sources)

    eye_lanes = (places[:, None] == places[None, :]).astype(jnp.float32)
    right_diag = jnp.sum(right_side * eye_lanes, axis=2)
    prefix_mix, prefix_blocks = prefix_scan(own_mix, own_blocks)
    mixed = channel_mix(prefix_mix, boundary)
    half = jnp.einsum("wkl,lj->wkj", mixed, prefix_blocks, precision=HIGH)
    left_env = jnp.einsum("ki,wkj->iwj", prefix_blocks, half, precision=HIGH)
    left_diag = jnp.sum(prefix_blocks[None] * half, axis=1)
    diagonal = jnp.einsum("wi,wj->ij", left_diag, right_diag, precision=HIGH)

    def apply_h(vector, moved):
        inner = jnp.einsum("iwj,jk->iwk", left_env, vector, precision=HIGH)
        local_part = jnp.einsum("iwk,wkl->il", inner, right_side, precision=HIGH)
        return masking * (local_part + product(left_hop, moved))

    def step(vector, image_vec, rayleigh):
        residue = image_vec - rayleigh * vector
        shifted = diagonal - rayleigh
        return vector - residue * shifted / (shifted * shifted + 1.0)

    image = apply_h(first, first_moved)
    sums = sec_total(jnp.stack([jnp.sum(first * first), jnp.sum(first * image)]))
    scale = 1.0 / jnp.sqrt(sums[0] + EPSILON)
    vector = first * scale
    image_vec = image * scale
    rayleigh = sums[1] / (sums[0] + EPSILON)
    for turn_index in range(1, DAV):
        update = step(vector, image_vec, rayleigh)
        moved = regroup(product(update, right_hop), all_sources)
        image = apply_h(update, moved)
        sums = sec_total(jnp.stack([jnp.sum(update * update), jnp.sum(update * image)]))
        scale = 1.0 / jnp.sqrt(sums[0] + EPSILON)
        vector = update * scale
        image_vec = image * scale
        rayleigh = sums[1] / (sums[0] + EPSILON)
    update = step(vector, image_vec, rayleigh)
    total = sec_total(jnp.sum(update * update)[None])[0]
    cells = float(sector_count * block_width * block_width)
    return (update * (jnp.sqrt(jnp.float32(cells)) / jnp.sqrt(total + EPSILON)))[None, None]


def solution(mesh):
    return jax.shard_map(
        per_device,
        mesh=mesh,
        in_specs=(
            P("seg", "sec", None, None),
            P("sec", None, None, None),
            P("seg", "sec", None, None, None),
            P("seg", "sec", None, None),
            P("seg", None, None),
            P("seg", "sec", None, None),
            P("seg", "sec", None, None),
            P("seg", None, None),
            P("seg", None),
        ),
        out_specs=P("seg", "sec", None, None),
        check_vma=False,
    )
```

```python
import jax
import jax.numpy as jnp
from jax import lax
from jax.sharding import PartitionSpec as P
from jax.experimental import pallas as pl
from jax.experimental.pallas import tpu as pltpu

DAV = 2


HIGH = lax.Precision.HIGHEST
EPSILON = 1e-06


def passed_along(value, axis, steps):
    count = lax.axis_size(axis)
    initial, last = (max(0, -steps), min(count, count - steps))
    return lax.ppermute(value, axis, [(source, source + steps) for source in range(initial, last)])


def product(left, right):
    return jnp.matmul(left, right, precision=HIGH)


def sec_total(values):
    count = lax.axis_size("sec")
    spread = jnp.broadcast_to(values[None, :], (count, values.shape[0]))
    return jnp.sum(lax.all_to_all(spread, "sec", 0, 0, tiled=True), axis=0)


def regroup(moving, wanted):
    count = lax.axis_size("sec")
    rows, cols = moving.shape
    pieces = moving.reshape(count, rows // count, cols)
    held = lax.all_to_all(pieces, "sec", 0, 0, tiled=True)
    ordered = jnp.take(held, wanted, axis=0, mode="clip")
    back = lax.all_to_all(ordered, "sec", 0, 0, tiled=True)
    return back.reshape(rows, cols)


def _mix_half_kernel(mix_ref, source_ref, blocks_ref, rows_ref, half_ref, diag_ref):
    channels = source_ref.shape[0]

    @pl.when(pl.program_id(0) == 0)
    def _():
        diag_ref[...] = jnp.zeros_like(diag_ref)

    blocks = blocks_ref[...]
    tile_rows = rows_ref[...]
    for w in range(channels):
        acc = source_ref[0] * mix_ref[0, w]
        for u in range(1, channels):
            acc = acc + source_ref[u] * mix_ref[u, w]
        part = jnp.dot(acc, blocks, precision=HIGH, preferred_element_type=jnp.float32)
        half_ref[w] = part
        diag_ref[w:w + 1, :] += jnp.sum(tile_rows * part, axis=0, keepdims=True)


def mix_and_half(mix, source, blocks, rows=64):
    channels, height, width = source.shape
    return pl.pallas_call(
        _mix_half_kernel,
        grid=(height // rows,),
        in_specs=[
            pl.BlockSpec(memory_space=pltpu.SMEM),
            pl.BlockSpec((channels, rows, width), lambda i: (0, i, 0)),
            pl.BlockSpec((height, width), lambda i: (0, 0)),
            pl.BlockSpec((rows, width), lambda i: (i, 0)),
        ],
        out_specs=[
            pl.BlockSpec((channels, rows, width), lambda i: (0, i, 0)),
            pl.BlockSpec((channels, width), lambda i: (0, 0)),
        ],
        out_shape=[
            jax.ShapeDtypeStruct(source.shape, source.dtype),
            jax.ShapeDtypeStruct((channels, width), source.dtype),
        ],
    )(mix, source, blocks, blocks)


def prefix_scan(own_mix, own_blocks):
    seg = lax.axis_index("seg")
    count = lax.axis_size("seg")
    width = own_blocks.shape[0]
    channels = own_mix.shape[0]
    pad = -(-channels // 8) * 8
    eye_mix = jnp.eye(channels, dtype=jnp.float32)
    eye_blocks = jnp.eye(width, dtype=jnp.float32)
    span_mix, span_blocks = own_mix, own_blocks
    before_mix, before_blocks = eye_mix, eye_blocks
    step = 1
    while step < count:
        packed = jnp.concatenate(
            [span_blocks, jnp.pad(span_mix, ((0, pad - channels), (0, width - channels)))], axis=0
        )
        got = passed_along(packed, "seg", step)
        got_blocks = got[:width]
        got_mix = got[width:width + channels, :channels]
        take = seg >= step
        if step == 1:
            before_mix = jnp.where(take, got_mix, eye_mix)
            before_blocks = jnp.where(take, got_blocks, eye_blocks)
        else:
            before_mix = jnp.where(take, product(got_mix, before_mix), before_mix)
            before_blocks = jnp.where(take, product(got_blocks, before_blocks), before_blocks)
        if step * 2 < count:
            span_mix = jnp.where(take, product(got_mix, span_mix), span_mix)
            span_blocks = jnp.where(take, product(got_blocks, span_blocks), span_blocks)
        step *= 2
    return before_mix, before_blocks


def per_device(
    psi_init,
    boundary_env,
    right_env,
    transfer_blocks,
    transfer_mix,
    hop_left,
    hop_right,
    block_sizes,
    sources,
):
    initial = psi_init[0, 0]
    boundary = boundary_env[0]
    right_side = right_env[0, 0]
    own_blocks = transfer_blocks[0, 0]
    own_mix = transfer_mix[0]
    left_hop = hop_left[0, 0]
    right_hop = hop_right[0, 0]
    all_sizes = block_sizes[0]
    all_sources = sources[0]
    block_width = initial.shape[1]
    sector_count = lax.axis_size("sec")
    me = lax.axis_index("sec")

    places = lax.broadcasted_iota(jnp.int32, (block_width,), 0)
    row_live = (places < all_sizes[0, me]).astype(jnp.float32)
    col_live = (places < all_sizes[1, me]).astype(jnp.float32)
    masking = row_live[:, None] * col_live[None, :]

    first = masking * initial
    first_moved = regroup(product(first, right_hop), all_sources)

    eye_lanes = (places[:, None] == places[None, :]).astype(jnp.float32)
    right_diag = jnp.sum(right_side * eye_lanes, axis=2)
    prefix_mix, prefix_blocks = prefix_scan(own_mix, own_blocks)
    half, left_diag = mix_and_half(prefix_mix, boundary, prefix_blocks)
    left_env = jnp.einsum("ki,wkj->iwj", prefix_blocks, half, precision=HIGH)
    diagonal = jnp.einsum("wi,wj->ij", left_diag, right_diag, precision=HIGH)

    def apply_h(vector, moved):
        inner = jnp.einsum("iwj,jk->iwk", left_env, vector, precision=HIGH)
        local_part = jnp.einsum("iwk,wkl->il", inner, right_side, precision=HIGH)
        return masking * (local_part + product(left_hop, moved))

    def step(vector, image_vec, rayleigh):
        residue = image_vec - rayleigh * vector
        shifted = diagonal - rayleigh
        return vector - residue * shifted / (shifted * shifted + 1.0)

    image = apply_h(first, first_moved)
    sums = sec_total(jnp.stack([jnp.sum(first * first), jnp.sum(first * image)]))
    scale = 1.0 / jnp.sqrt(sums[0] + EPSILON)
    vector = first * scale
    image_vec = image * scale
    rayleigh = sums[1] / (sums[0] + EPSILON)
    for turn_index in range(1, DAV):
        update = step(vector, image_vec, rayleigh)
        moved = regroup(product(update, right_hop), all_sources)
        image = apply_h(update, moved)
        sums = sec_total(jnp.stack([jnp.sum(update * update), jnp.sum(update * image)]))
        scale = 1.0 / jnp.sqrt(sums[0] + EPSILON)
        vector = update * scale
        image_vec = image * scale
        rayleigh = sums[1] / (sums[0] + EPSILON)
    update = step(vector, image_vec, rayleigh)
    total = sec_total(jnp.sum(update * update)[None])[0]
    cells = float(sector_count * block_width * block_width)
    return (update * (jnp.sqrt(jnp.float32(cells)) / jnp.sqrt(total + EPSILON)))[None, None]


def solution(mesh):
    return jax.shard_map(
        per_device,
        mesh=mesh,
        in_specs=(
            P("seg", "sec", None, None),
            P("sec", None, None, None),
            P("seg", "sec", None, None, None),
            P("seg", "sec", None, None),
            P("seg", None, None),
            P("seg", "sec", None, None),
            P("seg", "sec", None, None),
            P("seg", None, None),
            P("seg", None),
        ),
        out_specs=P("seg", "sec", None, None),
        check_vma=False,
    )
```

```python
import jax
import jax.numpy as jnp
from jax import lax
from jax.sharding import PartitionSpec as P
from jax.experimental import pallas as pl
from jax.experimental.pallas import tpu as pltpu

DAV = 2


HIGH = lax.Precision.HIGHEST
EPSILON = 1e-06


def passed_along(value, axis, steps):
    count = lax.axis_size(axis)
    initial, last = (max(0, -steps), min(count, count - steps))
    return lax.ppermute(value, axis, [(source, source + steps) for source in range(initial, last)])


def product(left, right):
    return jnp.matmul(left, right, precision=HIGH)


def sec_total(values):
    count = lax.axis_size("sec")
    spread = jnp.broadcast_to(values[None, :], (count, values.shape[0]))
    return jnp.sum(lax.all_to_all(spread, "sec", 0, 0, tiled=True), axis=0)


def regroup(moving, wanted):
    count = lax.axis_size("sec")
    rows, cols = moving.shape
    pieces = moving.reshape(count, rows // count, cols)
    held = lax.all_to_all(pieces, "sec", 0, 0, tiled=True)
    ordered = jnp.take(held, wanted, axis=0, mode="clip")
    back = lax.all_to_all(ordered, "sec", 0, 0, tiled=True)
    return back.reshape(rows, cols)


def _mix_kernel(mix_ref, source_ref, out_ref):
    channels, rows, width = source_ref.shape

    def body(t, carry):
        r = pl.multiple_of(t * 8, 8)
        parts = [source_ref[u, pl.ds(r, 8), :] for u in range(channels)]
        for w in range(channels):
            acc = parts[0] * mix_ref[0, w]
            for u in range(1, channels):
                acc = acc + parts[u] * mix_ref[u, w]
            out_ref[w, pl.ds(r, 8), :] = acc
        return carry

    lax.fori_loop(0, rows // 8, body, 0)


def channel_mix(mix, source, rows=64):
    channels, height, width = source.shape
    return pl.pallas_call(
        _mix_kernel,
        grid=(height // rows,),
        in_specs=[
            pl.BlockSpec(memory_space=pltpu.SMEM),
            pl.BlockSpec((channels, rows, width), lambda i: (0, i, 0)),
        ],
        out_specs=pl.BlockSpec((channels, rows, width), lambda i: (0, i, 0)),
        out_shape=jax.ShapeDtypeStruct(source.shape, source.dtype),
    )(mix, source)


def prefix_scan(own_mix, own_blocks):
    seg = lax.axis_index("seg")
    count = lax.axis_size("seg")
    width = own_blocks.shape[0]
    channels = own_mix.shape[0]
    pad = -(-channels // 8) * 8
    eye_mix = jnp.eye(channels, dtype=jnp.float32)
    eye_blocks = jnp.eye(width, dtype=jnp.float32)
    span_mix, span_blocks = own_mix, own_blocks
    before_mix, before_blocks = eye_mix, eye_blocks
    step = 1
    while step < count:
        packed = jnp.concatenate(
            [span_blocks, jnp.pad(span_mix, ((0, pad - channels), (0, width - channels)))], axis=0
        )
        got = passed_along(packed, "seg", step)
        got_blocks = got[:width]
        got_mix = got[width:width + channels, :channels]
        take = seg >= step
        if step == 1:
            before_mix = jnp.where(take, got_mix, eye_mix)
            before_blocks = jnp.where(take, got_blocks, eye_blocks)
        else:
            before_mix = jnp.where(take, product(got_mix, before_mix), before_mix)
            before_blocks = jnp.where(take, product(got_blocks, before_blocks), before_blocks)
        if step * 2 < count:
            span_mix = jnp.where(take, product(got_mix, span_mix), span_mix)
            span_blocks = jnp.where(take, product(got_blocks, span_blocks), span_blocks)
        step *= 2
    return before_mix, before_blocks


def per_device(
    psi_init,
    boundary_env,
    right_env,
    transfer_blocks,
    transfer_mix,
    hop_left,
    hop_right,
    block_sizes,
    sources,
):
    initial = psi_init[0, 0]
    boundary = boundary_env[0]
    right_side = right_env[0, 0]
    own_blocks = transfer_blocks[0, 0]
    own_mix = transfer_mix[0]
    left_hop = hop_left[0, 0]
    right_hop = hop_right[0, 0]
    all_sizes = block_sizes[0]
    all_sources = sources[0]
    block_width = initial.shape[1]
    sector_count = lax.axis_size("sec")
    me = lax.axis_index("sec")

    places = lax.broadcasted_iota(jnp.int32, (block_width,), 0)
    row_live = (places < all_sizes[0, me]).astype(jnp.float32)
    col_live = (places < all_sizes[1, me]).astype(jnp.float32)
    masking = row_live[:, None] * col_live[None, :]

    first = masking * initial
    first_moved = regroup(product(first, right_hop), all_sources)

    eye_lanes = (places[:, None] == places[None, :]).astype(jnp.float32)
    right_diag = jnp.sum(right_side * eye_lanes, axis=2)
    prefix_mix, prefix_blocks = prefix_scan(own_mix, own_blocks)
    mixed = channel_mix(prefix_mix, boundary)
    half = jnp.einsum("wkl,lj->wkj", mixed, prefix_blocks, precision=HIGH)
    left_env = jnp.einsum("ki,wkj->iwj", prefix_blocks, half, precision=HIGH)
    left_diag = jnp.sum(prefix_blocks[None] * half, axis=1)
    diagonal = jnp.einsum("wi,wj->ij", left_diag, right_diag, precision=HIGH)

    def apply_h(vector, moved):
        inner = jnp.einsum("iwj,jk->iwk", left_env, vector, precision=HIGH)
        local_part = jnp.einsum("iwk,wkl->il", inner, right_side, precision=HIGH)
        return masking * (local_part + product(left_hop, moved))

    def step(vector, image_vec, rayleigh):
        residue = image_vec - rayleigh * vector
        shifted = diagonal - rayleigh
        return vector - residue * shifted / (shifted * shifted + 1.0)

    image = apply_h(first, first_moved)
    sums = sec_total(jnp.stack([jnp.sum(first * first), jnp.sum(first * image)]))
    scale = 1.0 / jnp.sqrt(sums[0] + EPSILON)
    vector = first * scale
    image_vec = image * scale
    rayleigh = sums[1] / (sums[0] + EPSILON)
    for turn_index in range(1, DAV):
        update = step(vector, image_vec, rayleigh)
        moved = regroup(product(update, right_hop), all_sources)
        image = apply_h(update, moved)
        sums = sec_total(jnp.stack([jnp.sum(update * update), jnp.sum(update * image)]))
        scale = 1.0 / jnp.sqrt(sums[0] + EPSILON)
        vector = update * scale
        image_vec = image * scale
        rayleigh = sums[1] / (sums[0] + EPSILON)
    update = step(vector, image_vec, rayleigh)
    total = sec_total(jnp.sum(update * update)[None])[0]
    cells = float(sector_count * block_width * block_width)
    return (update * (jnp.sqrt(jnp.float32(cells)) / jnp.sqrt(total + EPSILON)))[None, None]


def solution(mesh):
    return jax.shard_map(
        per_device,
        mesh=mesh,
        in_specs=(
            P("seg", "sec", None, None),
            P("sec", None, None, None),
            P("seg", "sec", None, None, None),
            P("seg", "sec", None, None),
            P("seg", None, None),
            P("seg", "sec", None, None),
            P("seg", "sec", None, None),
            P("seg", None, None),
            P("seg", None),
        ),
        out_specs=P("seg", "sec", None, None),
        check_vma=False,
    )
```

```python
import jax
import jax.numpy as jnp
from jax import lax
from jax.sharding import PartitionSpec as P
from jax.experimental import pallas as pl
from jax.experimental.pallas import tpu as pltpu

DAV = 2


HIGH = lax.Precision.HIGHEST
EPSILON = 1e-06


def passed_along(value, axis, steps):
    count = lax.axis_size(axis)
    initial, last = (max(0, -steps), min(count, count - steps))
    return lax.ppermute(value, axis, [(source, source + steps) for source in range(initial, last)])


def product(left, right):
    return jnp.matmul(left, right, precision=HIGH)


def sec_total(values):
    count = lax.axis_size("sec")
    spread = jnp.broadcast_to(values[None, :], (count, values.shape[0]))
    return jnp.sum(lax.all_to_all(spread, "sec", 0, 0, tiled=True), axis=0)


def regroup(moving, wanted):
    count = lax.axis_size("sec")
    rows, cols = moving.shape
    pieces = moving.reshape(count, rows // count, cols)
    held = lax.all_to_all(pieces, "sec", 0, 0, tiled=True)
    ordered = jnp.take(held, wanted, axis=0, mode="clip")
    back = lax.all_to_all(ordered, "sec", 0, 0, tiled=True)
    return back.reshape(rows, cols)


def _mix_kernel(mix_ref, source_ref, out_ref):
    channels = source_ref.shape[0]
    for w in range(channels):
        acc = source_ref[0] * mix_ref[0, w]
        for u in range(1, channels):
            acc = acc + source_ref[u] * mix_ref[u, w]
        out_ref[w] = acc


def channel_mix(mix, source, rows=128):
    channels, height, width = source.shape
    return pl.pallas_call(
        _mix_kernel,
        grid=(height // rows,),
        in_specs=[
            pl.BlockSpec(memory_space=pltpu.SMEM),
            pl.BlockSpec((channels, rows, width), lambda i: (0, i, 0)),
        ],
        out_specs=pl.BlockSpec((channels, rows, width), lambda i: (0, i, 0)),
        out_shape=jax.ShapeDtypeStruct(source.shape, source.dtype),
    )(mix, source)


def prefix_scan(own_mix, own_blocks):
    seg = lax.axis_index("seg")
    count = lax.axis_size("seg")
    width = own_blocks.shape[0]
    channels = own_mix.shape[0]
    pad = -(-channels // 8) * 8
    eye_mix = jnp.eye(channels, dtype=jnp.float32)
    eye_blocks = jnp.eye(width, dtype=jnp.float32)
    span_mix, span_blocks = own_mix, own_blocks
    before_mix, before_blocks = eye_mix, eye_blocks
    step = 1
    while step < count:
        packed = jnp.concatenate(
            [span_blocks, jnp.pad(span_mix, ((0, pad - channels), (0, width - channels)))], axis=0
        )
        got = passed_along(packed, "seg", step)
        got_blocks = got[:width]
        got_mix = got[width:width + channels, :channels]
        take = seg >= step
        if step == 1:
            before_mix = jnp.where(take, got_mix, eye_mix)
            before_blocks = jnp.where(take, got_blocks, eye_blocks)
        else:
            before_mix = jnp.where(take, product(got_mix, before_mix), before_mix)
            before_blocks = jnp.where(take, product(got_blocks, before_blocks), before_blocks)
        if step * 2 < count:
            span_mix = jnp.where(take, product(got_mix, span_mix), span_mix)
            span_blocks = jnp.where(take, product(got_blocks, span_blocks), span_blocks)
        step *= 2
    return before_mix, before_blocks


def per_device(
    psi_init,
    boundary_env,
    right_env,
    transfer_blocks,
    transfer_mix,
    hop_left,
    hop_right,
    block_sizes,
    sources,
):
    initial = psi_init[0, 0]
    boundary = boundary_env[0]
    right_side = right_env[0, 0]
    own_blocks = transfer_blocks[0, 0]
    own_mix = transfer_mix[0]
    left_hop = hop_left[0, 0]
    right_hop = hop_right[0, 0]
    all_sizes = block_sizes[0]
    all_sources = sources[0]
    block_width = initial.shape[1]
    sector_count = lax.axis_size("sec")
    me = lax.axis_index("sec")

    places = lax.broadcasted_iota(jnp.int32, (block_width,), 0)
    row_live = (places < all_sizes[0, me]).astype(jnp.float32)
    col_live = (places < all_sizes[1, me]).astype(jnp.float32)
    masking = row_live[:, None] * col_live[None, :]

    first = masking * initial
    first_moved = regroup(product(first, right_hop), all_sources)

    eye_lanes = (places[:, None] == places[None, :]).astype(jnp.float32)
    right_diag = jnp.sum(right_side * eye_lanes, axis=2)
    prefix_mix, prefix_blocks = prefix_scan(own_mix, own_blocks)
    mixed = channel_mix(prefix_mix, boundary)
    half = jnp.einsum("wkl,lj->wkj", mixed, prefix_blocks, precision=HIGH)
    left_env = jnp.einsum("ki,wkj->iwj", prefix_blocks, half, precision=HIGH)
    left_diag = jnp.sum(prefix_blocks[None] * half, axis=1)
    diagonal = jnp.einsum("wi,wj->ij", left_diag, right_diag, precision=HIGH)

    def apply_h(vector, moved):
        inner = jnp.einsum("iwj,jk->iwk", left_env, vector, precision=HIGH)
        local_part = jnp.einsum("iwk,wkl->il", inner, right_side, precision=HIGH)
        return masking * (local_part + product(left_hop, moved))

    def step(vector, image_vec, rayleigh):
        residue = image_vec - rayleigh * vector
        shifted = diagonal - rayleigh
        return vector - residue * shifted / (shifted * shifted + 1.0)

    image = apply_h(first, first_moved)
    sums = sec_total(jnp.stack([jnp.sum(first * first), jnp.sum(first * image)]))
    scale = 1.0 / jnp.sqrt(sums[0] + EPSILON)
    vector = first * scale
    image_vec = image * scale
    rayleigh = sums[1] / (sums[0] + EPSILON)
    for turn_index in range(1, DAV):
        update = step(vector, image_vec, rayleigh)
        moved = regroup(product(update, right_hop), all_sources)
        image = apply_h(update, moved)
        sums = sec_total(jnp.stack([jnp.sum(update * update), jnp.sum(update * image)]))
        scale = 1.0 / jnp.sqrt(sums[0] + EPSILON)
        vector = update * scale
        image_vec = image * scale
        rayleigh = sums[1] / (sums[0] + EPSILON)
    update = step(vector, image_vec, rayleigh)
    total = sec_total(jnp.sum(update * update)[None])[0]
    cells = float(sector_count * block_width * block_width)
    return (update * (jnp.sqrt(jnp.float32(cells)) / jnp.sqrt(total + EPSILON)))[None, None]


def solution(mesh):
    return jax.shard_map(
        per_device,
        mesh=mesh,
        in_specs=(
            P("seg", "sec", None, None),
            P("sec", None, None, None),
            P("seg", "sec", None, None, None),
            P("seg", "sec", None, None),
            P("seg", None, None),
            P("seg", "sec", None, None),
            P("seg", "sec", None, None),
            P("seg", None, None),
            P("seg", None),
        ),
        out_specs=P("seg", "sec", None, None),
        check_vma=False,
    )
```

```python
import jax
import jax.numpy as jnp
from jax import lax
from jax.sharding import PartitionSpec as P
from jax.experimental import pallas as pl
from jax.experimental.pallas import tpu as pltpu

DAV = 2


HIGH = lax.Precision.HIGHEST
EPSILON = 1e-06


def passed_along(value, axis, steps):
    count = lax.axis_size(axis)
    initial, last = (max(0, -steps), min(count, count - steps))
    return lax.ppermute(value, axis, [(source, source + steps) for source in range(initial, last)])


def product(left, right):
    return jnp.matmul(left, right, precision=HIGH)


def sec_total(values):
    count = lax.axis_size("sec")
    spread = jnp.broadcast_to(values[None, :], (count, values.shape[0]))
    return jnp.sum(lax.all_to_all(spread, "sec", 0, 0, tiled=True), axis=0)


def regroup(moving, wanted):
    count = lax.axis_size("sec")
    rows, cols = moving.shape
    pieces = moving.reshape(count, rows // count, cols)
    held = lax.all_to_all(pieces, "sec", 0, 0, tiled=True)
    chooser = (wanted[:, None] == lax.broadcasted_iota(jnp.int32, (1, count), 1)).astype(held.dtype)
    ordered = jnp.einsum("bc,cpq->bpq", chooser, held, precision=HIGH)
    back = lax.all_to_all(ordered, "sec", 0, 0, tiled=True)
    return back.reshape(rows, cols)


def _mix_kernel(mix_ref, source_ref, out_ref):
    channels = source_ref.shape[0]
    for w in range(channels):
        acc = source_ref[0] * mix_ref[0, w]
        for u in range(1, channels):
            acc = acc + source_ref[u] * mix_ref[u, w]
        out_ref[w] = acc


def channel_mix(mix, source, rows=64):
    channels, height, width = source.shape
    return pl.pallas_call(
        _mix_kernel,
        grid=(height // rows,),
        in_specs=[
            pl.BlockSpec(memory_space=pltpu.SMEM),
            pl.BlockSpec((channels, rows, width), lambda i: (0, i, 0)),
        ],
        out_specs=pl.BlockSpec((channels, rows, width), lambda i: (0, i, 0)),
        out_shape=jax.ShapeDtypeStruct(source.shape, source.dtype),
    )(mix, source)


def prefix_scan(own_mix, own_blocks):
    seg = lax.axis_index("seg")
    count = lax.axis_size("seg")
    width = own_blocks.shape[0]
    channels = own_mix.shape[0]
    pad = -(-channels // 8) * 8
    eye_mix = jnp.eye(channels, dtype=jnp.float32)
    eye_blocks = jnp.eye(width, dtype=jnp.float32)
    span_mix, span_blocks = own_mix, own_blocks
    before_mix, before_blocks = eye_mix, eye_blocks
    step = 1
    while step < count:
        packed = jnp.concatenate(
            [span_blocks, jnp.pad(span_mix, ((0, pad - channels), (0, width - channels)))], axis=0
        )
        got = passed_along(packed, "seg", step)
        got_blocks = got[:width]
        got_mix = got[width:width + channels, :channels]
        take = seg >= step
        if step == 1:
            before_mix = jnp.where(take, got_mix, eye_mix)
            before_blocks = jnp.where(take, got_blocks, eye_blocks)
        else:
            before_mix = jnp.where(take, product(got_mix, before_mix), before_mix)
            before_blocks = jnp.where(take, product(got_blocks, before_blocks), before_blocks)
        if step * 2 < count:
            span_mix = jnp.where(take, product(got_mix, span_mix), span_mix)
            span_blocks = jnp.where(take, product(got_blocks, span_blocks), span_blocks)
        step *= 2
    return before_mix, before_blocks


def per_device(
    psi_init,
    boundary_env,
    right_env,
    transfer_blocks,
    transfer_mix,
    hop_left,
    hop_right,
    block_sizes,
    sources,
):
    initial = psi_init[0, 0]
    boundary = boundary_env[0]
    right_side = right_env[0, 0]
    own_blocks = transfer_blocks[0, 0]
    own_mix = transfer_mix[0]
    left_hop = hop_left[0, 0]
    right_hop = hop_right[0, 0]
    all_sizes = block_sizes[0]
    all_sources = sources[0]
    block_width = initial.shape[1]
    sector_count = lax.axis_size("sec")
    me = lax.axis_index("sec")

    places = lax.broadcasted_iota(jnp.int32, (block_width,), 0)
    row_live = (places < all_sizes[0, me]).astype(jnp.float32)
    col_live = (places < all_sizes[1, me]).astype(jnp.float32)
    masking = row_live[:, None] * col_live[None, :]

    first = masking * initial
    first_moved = regroup(product(first, right_hop), all_sources)

    eye_lanes = (places[:, None] == places[None, :]).astype(jnp.float32)
    right_diag = jnp.sum(right_side * eye_lanes, axis=2)
    prefix_mix, prefix_blocks = prefix_scan(own_mix, own_blocks)
    mixed = channel_mix(prefix_mix, boundary)
    half = jnp.einsum("wkl,lj->wkj", mixed, prefix_blocks, precision=HIGH)
    left_env = jnp.einsum("ki,wkj->iwj", prefix_blocks, half, precision=HIGH)
    left_diag = jnp.sum(prefix_blocks[None] * half, axis=1)
    diagonal = jnp.einsum("wi,wj->ij", left_diag, right_diag, precision=HIGH)

    def apply_h(vector, moved):
        inner = jnp.einsum("iwj,jk->iwk", left_env, vector, precision=HIGH)
        local_part = jnp.einsum("iwk,wkl->il", inner, right_side, precision=HIGH)
        return masking * (local_part + product(left_hop, moved))

    def step(vector, image_vec, rayleigh):
        residue = image_vec - rayleigh * vector
        shifted = diagonal - rayleigh
        return vector - residue * shifted / (shifted * shifted + 1.0)

    image = apply_h(first, first_moved)
    sums = sec_total(jnp.stack([jnp.sum(first * first), jnp.sum(first * image)]))
    scale = 1.0 / jnp.sqrt(sums[0] + EPSILON)
    vector = first * scale
    image_vec = image * scale
    rayleigh = sums[1] / (sums[0] + EPSILON)
    for turn_index in range(1, DAV):
        update = step(vector, image_vec, rayleigh)
        moved = regroup(product(update, right_hop), all_sources)
        image = apply_h(update, moved)
        sums = sec_total(jnp.stack([jnp.sum(update * update), jnp.sum(update * image)]))
        scale = 1.0 / jnp.sqrt(sums[0] + EPSILON)
        vector = update * scale
        image_vec = image * scale
        rayleigh = sums[1] / (sums[0] + EPSILON)
    update = step(vector, image_vec, rayleigh)
    total = sec_total(jnp.sum(update * update)[None])[0]
    cells = float(sector_count * block_width * block_width)
    return (update * (jnp.sqrt(jnp.float32(cells)) / jnp.sqrt(total + EPSILON)))[None, None]


def solution(mesh):
    return jax.shard_map(
        per_device,
        mesh=mesh,
        in_specs=(
            P("seg", "sec", None, None),
            P("sec", None, None, None),
            P("seg", "sec", None, None, None),
            P("seg", "sec", None, None),
            P("seg", None, None),
            P("seg", "sec", None, None),
            P("seg", "sec", None, None),
            P("seg", None, None),
            P("seg", None),
        ),
        out_specs=P("seg", "sec", None, None),
        check_vma=False,
    )
```
